256 devices in a mesh: dp: 32 (over x, z), own: 8 (over y, core).
Axes of the slice: x: 4, y: 4, z: 8, core: 2. Of those that a mesh axis runs over, the one named last changes fastest.
Arguments:
- partials: bfloat16 [32, 64, 256, 1024], P('dp', None, None, 'own')
- owner: int32 [64, 1], replicated, may hold values from 0 to 31; in each aligned block of 64 rows (0 to 63, 64 to 127, ...) at most 4 rows name the same one
- momentum: float32 [32, 4, 256, 1024], P('dp', None, None, 'own'), may hold values from -1.2 to 1.2
- master: float32 [32, 4, 256, 1024], P('dp', None, None, 'own'), may hold values from -0.3 to 0.3
Outputs:
- new_momentum: float32 [32, 4, 256, 1024], P('dp', None, None, 'own')
- new_master: float32 [32, 4, 256, 1024], P('dp', None, None, 'own')
- new_weights: bfloat16 [64, 256, 1024], P(None, None, 'own')
The draws below stay inside these ranges and needn't reach their ends.
Inputs may be any that keep to these rules, and one draw needn't show every extreme that they name: `owner`: every group owns at least one block and at most 4 blocks; some group owns exactly 4.
All inputs are finite; a program needn't handle non-finite values.
Results may differ from the reference program's by a relative error of at most 0.0007.
Values may be sent and summed in bfloat16 or wider, within the bound.
No kernel may reach another device: no remote copies, remote signals or barrier semaphores. Data moves between devices by JAX's collectives and lax.ppermute only.
A program may use at most 128 MiB of HBM per device.

```python
import math
import jax
import jax.numpy as jnp
import numpy as np
from jax import lax

D = 1024
R = 256
ITERS = 5
GROUPS = 32
NBLK = 64
SLOTS = 4


def draw_partials(key, part):
    keys = jax.random.split(key, 5)
    shape = (GROUPS, NBLK, R, D)
    base = jax.random.normal(keys[0], shape, jnp.float32)
    row_span = math.log(10.0)
    ramp_span = math.log(30.0)
    row_scale = jnp.exp(jax.random.uniform(keys[2], (1, NBLK, R, 1), jnp.float32, 0.0, row_span)) / 3.0
    ramp = jnp.arange(D, dtype=jnp.float32) * (ramp_span / (D - 1))
    col_scale = jnp.exp(jax.random.uniform(keys[3], (D,), jnp.float32, 0.0, math.log(10.0)) + ramp) / 20.0
    pair = jnp.exp(jax.random.uniform(keys[4], (GROUPS, NBLK, 1, 1), jnp.float32, math.log(0.3), math.log(3.0)))
    values = base * row_scale * col_scale.reshape(1, 1, 1, D) * pair * (1.0 / math.sqrt(GROUPS))
    return values.astype(jnp.bfloat16)


def shard_levels(own_key, extent, cuts, smallest, top_value):
    def one(axis_at, shards_of):
        steps = jax.random.uniform(jax.random.fold_in(jax.random.fold_in(own_key, 6), axis_at), (shards_of,), jnp.float32, smallest / len(cuts), top_value / len(cuts))
        return jnp.repeat(jnp.exp(steps), extent[axis_at] // shards_of).reshape((-1,) + (1,) * (len(extent) - axis_at - 1))

    gain = one(*cuts[0])
    for cut in cuts[1:]:
        gain = gain * one(*cut)
    return gain


def routed_block(own_key, own, number, rows, amount, top, most, skew):
    ranking = jax.random.permutation(own_key, amount)
    packed, usual = portions_of(amount, rows * top, most, skew, True), portions_of(amount, rows * top, most, skew, False)
    places = jnp.arange(amount)

    def named(lengths, rotation):
        used = int((lengths > 0).sum())
        fixed = max(1, used // 4)
        moved = fixed + (places - fixed + rotation * (used - fixed)) % max(1, amount - fixed)
        return jnp.zeros((amount,), jnp.int32).at[ranking[jnp.where(places < fixed, places, moved)]].set(jnp.asarray(lengths, jnp.int32))

    lengths = jnp.where(number % 4 == 0, named(packed, number // 4), named(usual, number - number // 4 - 1))
    mixed = jax.random.permutation(jax.random.fold_in(own, 3), amount)
    source_of, taker = mixed[0:amount // 2 * 2:2], mixed[1:amount // 2 * 2:2]
    slack = jnp.minimum(lengths[source_of] - 1, most - lengths[taker]) // 2
    slack = jnp.where((source_of == ranking[0]) | (taker == ranking[0]) | (lengths[taker] == 0), 0, jnp.maximum(slack, 0))
    moved = jax.random.randint(jax.random.fold_in(own, 4), (amount // 2,), 0, 1 << 20) % (slack + 1)
    lengths = lengths.at[source_of].add(-moved).at[taker].add(moved)
    labels = jnp.searchsorted(jnp.cumsum(lengths), jnp.arange(rows * top), side="right").astype(jnp.int32)
    table = labels.reshape(top, rows).T
    table = table[jax.random.permutation(jax.random.fold_in(own, 1), rows)]
    rotation = jax.random.randint(jax.random.fold_in(own, 2), (rows, 1), 0, top)
    return jnp.take_along_axis(table, (jnp.arange(top)[None, :] + rotation) % top, axis=1)


def portions_of(count, total, reach, slope, full):
    loads = [(1 << 20) // math.isqrt(rank ** slope) + 1 for rank in range(1, count + 1)]
    largest = reach if full else min(reach, max(-(-total // count), total * loads[0] // sum(loads)))
    least = 1 if total - largest >= count - 1 else 0
    counts, surplus = [largest] + [least] * (count - 1), total - largest - least * (count - 1)
    while surplus > 0:
        movable = [i for i in range(1, count) if counts[i] < largest] or [i for i in range(1, count) if counts[i] < reach]
        pool, budget = sum([loads[i] for i in movable]), surplus
        for i in movable:
            addition = min(reach - counts[i], max(1, budget * loads[i] // pool), surplus)
            counts[i] = counts[i] + addition
            surplus = surplus - addition
    return np.array(counts)


def gaussian(stream_key, dims, width, most, cuts=(), kind=jnp.bfloat16):
    entries = jax.random.normal(stream_key, dims, jnp.float32) * width
    if len(cuts) > 0:
        entries = shard_levels(stream_key, dims, cuts, -0.22, 0.18) * entries
    return jnp.clip(entries, min=-most, max=most).astype(kind)


def setup_inputs(seed: int = 0) -> dict:
    arg_keys = jax.random.split(jax.random.key(seed), 5)
    partials = draw_partials(jax.random.fold_in(arg_keys[4], 71), 0)
    owner_keys = jax.random.split(jax.random.fold_in(arg_keys[1], 1), NBLK // NBLK)
    owner_turns = jax.random.permutation(jax.random.fold_in(arg_keys[1], 3), NBLK // NBLK)
    owner = jax.vmap(lambda own, number: routed_block(jax.random.fold_in(arg_keys[1], 2), own, number, NBLK, GROUPS, 1, SLOTS, 2))(owner_keys, owner_turns).reshape((NBLK, 1))
    momentum = gaussian(arg_keys[2], (GROUPS, SLOTS, R, D), 0.2, 1.2, ((0, 32), (3, 8)), jnp.float32)
    master = gaussian(arg_keys[3], (GROUPS, SLOTS, R, D), 0.05, 0.3, ((0, 32), (3, 8)), jnp.float32)
    return {"partials": partials, "owner": owner, "momentum": momentum, "master": master}


COEF_A = 3.4445
COEF_B = -4.775
COEF_C = 2.0315
BETA = 0.95
STEP_SIZE = 0.2
DECAY = 0.1
EPSILON = 1e-07

def slot_targets(owner_list, group_count, slot_count):
    onehot = (owner_list[:, None] == jnp.arange(group_count, dtype=jnp.int32)[None, :]).astype(jnp.int32)
    before = jnp.cumsum(onehot, axis=0) - onehot
    ranks = lax.optimization_barrier(jnp.sum(before * onehot, axis=1)).astype(jnp.int32)
    return (owner_list * slot_count + ranks).astype(jnp.int32)

def muon_slot(items):
    gradient, momentum_old, master_old = items
    momentum_new = BETA * momentum_old + gradient
    update = gradient + BETA * momentum_new
    scale = jnp.sqrt(jnp.sum(update * update)) + EPSILON
    ortho = update / scale
    for iteration in range(ITERS):
        gram = jnp.dot(ortho, ortho.T, precision=lax.Precision.HIGHEST, preferred_element_type=jnp.float32)
        square = jnp.dot(gram, gram, precision=lax.Precision.HIGHEST, preferred_element_type=jnp.float32)
        poly = COEF_B * gram + COEF_C * square
        ortho = COEF_A * ortho + jnp.dot(poly, ortho, precision=lax.Precision.HIGHEST, preferred_element_type=jnp.float32)
    factor = STEP_SIZE * 0.2 * math.sqrt(max(R, D))
    master_new = master_old * (1.0 - STEP_SIZE * DECAY) - factor * ortho
    return (momentum_new, master_new)

def reference(partials, owner, momentum, master):

    def add_part(total, piece):
        return (total + piece.astype(jnp.float32), None)
    grad_blocks, unused = lax.scan(add_part, jnp.zeros((NBLK, R, D), jnp.float32), partials)
    target = slot_targets(owner[:, 0].astype(jnp.int32), GROUPS, SLOTS)
    slot_grad = jnp.zeros((GROUPS * SLOTS, R, D), jnp.float32).at[target].set(grad_blocks)
    momentum_new, master_new = lax.map(muon_slot, (slot_grad, momentum.reshape(GROUPS * SLOTS, R, D), master.reshape(GROUPS * SLOTS, R, D)))
    weights = master_new[target].astype(jnp.bfloat16)
    return (momentum_new.reshape(GROUPS, SLOTS, R, D), master_new.reshape(GROUPS, SLOTS, R, D), weights)
```

```python
import math

import jax
import jax.numpy as jnp
from jax import lax
from jax.sharding import PartitionSpec as P

D = 1024
ITERS = 5


COEF_A = 3.4445
COEF_B = -4.775
COEF_C = 2.0315
BETA = 0.95
STEP_SIZE = 0.2
DECAY = 0.1
EPSILON = 1e-07


def slot_targets(owner_list, group_count, slot_count):
    onehot = (owner_list[:, None] == jnp.arange(group_count, dtype=jnp.int32)[None, :]).astype(
        jnp.int32
    )
    before = jnp.cumsum(onehot, axis=0) - onehot
    ranks = jnp.sum(before * onehot, axis=1)
    return owner_list * slot_count + ranks


def slot_sources(target, slot_count, block_count):
    positions = jnp.arange(slot_count, dtype=jnp.int32)
    matches = positions[:, None] == target[None, :]
    present = jnp.any(matches, axis=1)
    source = jnp.sum(
        jnp.where(matches, jnp.arange(block_count, dtype=jnp.int32)[None, :], 0), axis=1
    )
    return (present, source)


def local_gram(values):
    return jnp.einsum(
        "srk,stk->srt",
        values,
        values,
        precision=lax.Precision.HIGHEST,
        preferred_element_type=jnp.float32,
    )


def gram_total(values):
    return lax.psum(local_gram(values), "own")


def matmul(left, right):
    return jnp.einsum(
        "srt,stu->sru",
        left,
        right,
        precision=lax.Precision.HIGHEST,
        preferred_element_type=jnp.float32,
    )


def newton_turn(ortho, gram, eye, next_gram):
    square = matmul(gram, gram)
    poly = COEF_B * gram + COEF_C * square
    product = jnp.einsum(
        "srt,stk->srk",
        poly,
        ortho,
        precision=lax.Precision.HIGHEST,
        preferred_element_type=jnp.float32,
    )
    ortho = COEF_A * ortho + product
    if next_gram:
        step = COEF_A * eye + poly
        gram = matmul(step, matmul(gram, step))
    return ortho, gram


def on_device(partials, owner, momentum, master):
    group_count = lax.axis_size("dp")
    local_rows = partials[0]
    block_count = local_rows.shape[0]
    slot_count = momentum.shape[1]
    block_rows = momentum.shape[2]
    owner_list = owner[:, 0]
    target = slot_targets(owner_list, group_count, slot_count)
    present, source = slot_sources(target, group_count * slot_count, block_count)
    outgoing = jnp.where(
        present[:, None, None], jnp.take(local_rows, source, axis=0).astype(jnp.float32), 0.0
    )
    gradient = lax.psum_scatter(outgoing, "dp", scatter_dimension=0, tiled=True)
    momentum_new = BETA * momentum[0] + gradient
    update = gradient + BETA * momentum_new
    update_gram = gram_total(update)
    squares = jnp.trace(update_gram, axis1=1, axis2=2)
    factor = 1.0 / (jnp.sqrt(squares) + EPSILON)
    ortho = update * factor[:, None, None]
    gram = update_gram * (factor * factor)[:, None, None]
    eye = jnp.eye(block_rows, dtype=jnp.float32)[None]
    for iteration in range(ITERS):
        ortho, gram = newton_turn(ortho, gram, eye, iteration < ITERS - 1)
    step_factor = STEP_SIZE * 0.2 * math.sqrt(max(block_rows, D))
    master_new = master[0] * (1.0 - STEP_SIZE * DECAY) - step_factor * ortho
    weights_low = master_new.astype(jnp.bfloat16)
    every_slot = lax.all_gather(weights_low, "dp", axis=0, tiled=True)
    weights = jnp.take(every_slot, target, axis=0)
    return (momentum_new[None], master_new[None], weights)


def solution(mesh):
    in_specs = (
        P("dp", None, None, "own"),
        P(),
        P("dp", None, None, "own"),
        P("dp", None, None, "own"),
    )
    out_specs = (P("dp", None, None, "own"), P("dp", None, None, "own"), P(None, None, "own"))
    return jax.shard_map(
        on_device, mesh=mesh, in_specs=in_specs, out_specs=out_specs, check_vma=False
    )
```

```python
import math

import jax
import jax.numpy as jnp
from jax import lax
from jax.sharding import Mesh, PartitionSpec as P

D = 1024
ITERS = 5


COEF_A = 3.4445
COEF_B = -4.775
COEF_C = 2.0315
BETA = 0.95
STEP_SIZE = 0.2
DECAY = 0.1
EPSILON = 1e-07


def slot_targets(owner_list, group_count, slot_count):
    onehot = (owner_list[:, None] == jnp.arange(group_count, dtype=jnp.int32)[None, :]).astype(
        jnp.int32
    )
    before = jnp.cumsum(onehot, axis=0) - onehot
    ranks = jnp.sum(before * onehot, axis=1)
    return owner_list * slot_count + ranks


def slot_sources(target, slot_count, block_count):
    positions = jnp.arange(slot_count, dtype=jnp.int32)
    matches = positions[:, None] == target[None, :]
    present = jnp.any(matches, axis=1)
    source = jnp.sum(
        jnp.where(matches, jnp.arange(block_count, dtype=jnp.int32)[None, :], 0), axis=1
    )
    return (present, source)


def local_gram(values):
    return jnp.einsum(
        "srk,stk->srt",
        values,
        values,
        precision=lax.Precision.HIGHEST,
        preferred_element_type=jnp.float32,
    )


def gram_total(values):
    return lax.psum(local_gram(values), "own")


def matmul(left, right):
    return jnp.einsum(
        "srt,stu->sru",
        left,
        right,
        precision=lax.Precision.HIGHEST,
        preferred_element_type=jnp.float32,
    )


def newton_turn(ortho, gram, eye, next_gram):
    square = matmul(gram, gram)
    poly = COEF_B * gram + COEF_C * square
    product = jnp.einsum(
        "srt,stk->srk",
        poly,
        ortho,
        precision=lax.Precision.HIGHEST,
        preferred_element_type=jnp.float32,
    )
    ortho = COEF_A * ortho + product
    if next_gram:
        step = COEF_A * eye + poly
        gram = matmul(step, matmul(gram, step))
    return ortho, gram


def on_device(partials, owner, momentum, master):
    group_count = lax.axis_size("x") * lax.axis_size("z")
    local_rows = partials[0]
    block_count = local_rows.shape[0]
    slot_count = momentum.shape[1]
    block_rows = momentum.shape[2]
    owner_list = owner[:, 0]
    target = slot_targets(owner_list, group_count, slot_count)
    present, source = slot_sources(target, group_count * slot_count, block_count)
    outgoing = jnp.where(present[:, None, None], jnp.take(local_rows, source, axis=0), 0)
    row_count = lax.axis_size("x")
    outgoing = outgoing.reshape((row_count, -1) + outgoing.shape[1:])
    arrived = lax.all_to_all(outgoing, "x", 0, 0, tiled=True)
    row_sum = jnp.sum(arrived.astype(jnp.float32), axis=0)
    gradient = lax.psum_scatter(row_sum, "z", scatter_dimension=0, tiled=True)
    momentum_new = BETA * momentum[0] + gradient
    update = gradient + BETA * momentum_new
    update_gram = gram_total(update)
    squares = jnp.trace(update_gram, axis1=1, axis2=2)
    factor = 1.0 / (jnp.sqrt(squares) + EPSILON)
    ortho = update * factor[:, None, None]
    gram = update_gram * (factor * factor)[:, None, None]
    eye = jnp.eye(block_rows, dtype=jnp.float32)[None]
    for iteration in range(ITERS):
        ortho, gram = newton_turn(ortho, gram, eye, iteration < ITERS - 1)
    step_factor = STEP_SIZE * 0.2 * math.sqrt(max(block_rows, D))
    master_new = master[0] * (1.0 - STEP_SIZE * DECAY) - step_factor * ortho
    weights_low = master_new.astype(jnp.bfloat16)
    every_slot = lax.all_gather(weights_low, ("x", "z"), axis=0, tiled=True)
    weights = jnp.take(every_slot, target, axis=0)
    return (momentum_new[None], master_new[None], weights)


def split_mesh(mesh):
    devices = mesh.devices
    row_count = len({device.coords[0] for device in devices[:, 0]})
    shape = (row_count, devices.shape[0] // row_count, devices.shape[1])
    return Mesh(devices.reshape(shape), ("x", "z", "own"))


def solution(mesh):
    grid = split_mesh(mesh)
    data = ("x", "z")
    in_specs = (
        P(data, None, None, "own"),
        P(),
        P(data, None, None, "own"),
        P(data, None, None, "own"),
    )
    out_specs = (P(data, None, None, "own"), P(data, None, None, "own"), P(None, None, "own"))
    return jax.shard_map(
        on_device, mesh=grid, in_specs=in_specs, out_specs=out_specs, check_vma=False
    )
```

```python
import math

import jax
import jax.numpy as jnp
from jax import lax
from jax.sharding import Mesh, PartitionSpec as P

D = 1024
ITERS = 5


COEF_A = 3.4445
COEF_B = -4.775
COEF_C = 2.0315
BETA = 0.95
STEP_SIZE = 0.2
DECAY = 0.1
EPSILON = 1e-07


def slot_targets(owner_list, group_count, slot_count):
    onehot = (owner_list[:, None] == jnp.arange(group_count, dtype=jnp.int32)[None, :]).astype(
        jnp.int32
    )
    before = jnp.cumsum(onehot, axis=0) - onehot
    ranks = jnp.sum(before * onehot, axis=1)
    return owner_list * slot_count + ranks


def slot_sources(target, slot_count, block_count):
    positions = jnp.arange(slot_count, dtype=jnp.int32)
    matches = positions[:, None] == target[None, :]
    present = jnp.any(matches, axis=1)
    source = jnp.sum(
        jnp.where(matches, jnp.arange(block_count, dtype=jnp.int32)[None, :], 0), axis=1
    )
    return (present, source)


def local_gram(values):
    return jnp.einsum(
        "srk,stk->srt",
        values,
        values,
        precision=lax.Precision.HIGHEST,
        preferred_element_type=jnp.float32,
    )


def own_sum(total):
    size = lax.axis_size("own")
    index = lax.axis_index("own")
    bits = []
    bit = 1
    while bit < size:
        bits.append(bit)
        bit *= 2
    for bit in bits:
        high = (index & bit) != 0
        half = total.shape[1] // 2
        lower, upper = total[:, :half], total[:, half:]
        keep = jnp.where(high, upper, lower)
        send = jnp.where(high, lower, upper)
        pairs = [(i, i ^ bit) for i in range(size)]
        total = keep + lax.ppermute(send, "own", pairs)
    for bit in reversed(bits):
        high = (index & bit) != 0
        pairs = [(i, i ^ bit) for i in range(size)]
        other = lax.ppermute(total, "own", pairs)
        total = jnp.where(high, jnp.concatenate([other, total], axis=1), jnp.concatenate([total, other], axis=1))
    return total


def gram_total(values):
    return own_sum(local_gram(values))


def matmul(left, right):
    return jnp.einsum(
        "srt,stu->sru",
        left,
        right,
        precision=lax.Precision.HIGHEST,
        preferred_element_type=jnp.float32,
    )


def newton_turn(ortho, gram, eye, next_gram):
    square = matmul(gram, gram)
    poly = COEF_B * gram + COEF_C * square
    product = jnp.einsum(
        "srt,stk->srk",
        poly,
        ortho,
        precision=lax.Precision.HIGHEST,
        preferred_element_type=jnp.float32,
    )
    ortho = COEF_A * ortho + product
    if next_gram:
        step = COEF_A * eye + poly
        gram = matmul(step, matmul(gram, step))
    return ortho, gram


def on_device(partials, owner, momentum, master):
    group_count = lax.axis_size("x") * lax.axis_size("z")
    local_rows = partials[0]
    block_count = local_rows.shape[0]
    slot_count = momentum.shape[1]
    block_rows = momentum.shape[2]
    owner_list = owner[:, 0]
    target = slot_targets(owner_list, group_count, slot_count)
    present, source = slot_sources(target, group_count * slot_count, block_count)
    outgoing = jnp.where(present[:, None, None], jnp.take(local_rows, source, axis=0), 0)
    row_count = lax.axis_size("x")
    outgoing = outgoing.reshape((row_count, -1) + outgoing.shape[1:])
    arrived = lax.all_to_all(outgoing, "x", 0, 0, tiled=True)
    row_sum = jnp.sum(arrived.astype(jnp.float32), axis=0)
    gradient = lax.psum_scatter(row_sum, "z", scatter_dimension=0, tiled=True)
    momentum_new = BETA * momentum[0] + gradient
    update = gradient + BETA * momentum_new
    update_gram = gram_total(update)
    squares = jnp.trace(update_gram, axis1=1, axis2=2)
    factor = 1.0 / (jnp.sqrt(squares) + EPSILON)
    ortho = update * factor[:, None, None]
    gram = update_gram * (factor * factor)[:, None, None]
    eye = jnp.eye(block_rows, dtype=jnp.float32)[None]
    ortho, gram = lax.fori_loop(
        0, ITERS - 1, lambda _, carry: newton_turn(*carry, eye, True), (ortho, gram)
    )
    ortho, gram = newton_turn(ortho, gram, eye, False)
    step_factor = STEP_SIZE * 0.2 * math.sqrt(max(block_rows, D))
    master_new = master[0] * (1.0 - STEP_SIZE * DECAY) - step_factor * ortho
    weights_low = master_new.astype(jnp.bfloat16)
    every_slot = lax.all_gather(weights_low, ("x", "z"), axis=0, tiled=True)
    weights = jnp.take(every_slot, target, axis=0)
    return (momentum_new[None], master_new[None], weights)


def split_mesh(mesh):
    devices = mesh.devices
    row_count = len({device.coords[0] for device in devices[:, 0]})
    shape = (row_count, devices.shape[0] // row_count, devices.shape[1])
    return Mesh(devices.reshape(shape), ("x", "z", "own"))


def solution(mesh):
    grid = split_mesh(mesh)
    data = ("x", "z")
    in_specs = (
        P(data, None, None, "own"),
        P(),
        P(data, None, None, "own"),
        P(data, None, None, "own"),
    )
    out_specs = (P(data, None, None, "own"), P(data, None, None, "own"), P(None, None, "own"))
    return jax.shard_map(
        on_device, mesh=grid, in_specs=in_specs, out_specs=out_specs, check_vma=False
    )
```

```python
import math

import jax
import jax.numpy as jnp
from jax import lax
from jax.sharding import Mesh, PartitionSpec as P

D = 1024
ITERS = 5


COEF_A = 3.4445
COEF_B = -4.775
COEF_C = 2.0315
BETA = 0.95
STEP_SIZE = 0.2
DECAY = 0.1
EPSILON = 1e-07


def slot_targets(owner_list, group_count, slot_count):
    onehot = (owner_list[:, None] == jnp.arange(group_count, dtype=jnp.int32)[None, :]).astype(
        jnp.int32
    )
    before = jnp.cumsum(onehot, axis=0) - onehot
    ranks = jnp.sum(before * onehot, axis=1)
    return owner_list * slot_count + ranks


def slot_sources(target, slot_count, block_count):
    positions = jnp.arange(slot_count, dtype=jnp.int32)
    matches = positions[:, None] == target[None, :]
    present = jnp.any(matches, axis=1)
    source = jnp.sum(
        jnp.where(matches, jnp.arange(block_count, dtype=jnp.int32)[None, :], 0), axis=1
    )
    return (present, source)


def local_gram(values):
    return jnp.einsum(
        "srk,stk->srt",
        values,
        values,
        precision=lax.Precision.HIGHEST,
        preferred_element_type=jnp.float32,
    )


def own_sum(total):
    size = lax.axis_size("own")
    index = lax.axis_index("own")
    bits = []
    bit = 1
    while bit < size:
        bits.append(bit)
        bit *= 2
    for bit in bits:
        high = (index & bit) != 0
        half = total.shape[1] // 2
        lower, upper = total[:, :half], total[:, half:]
        keep = jnp.where(high, upper, lower)
        send = jnp.where(high, lower, upper)
        pairs = [(i, i ^ bit) for i in range(size)]
        total = keep + lax.ppermute(send, "own", pairs)
    for bit in reversed(bits):
        high = (index & bit) != 0
        pairs = [(i, i ^ bit) for i in range(size)]
        other = lax.ppermute(total, "own", pairs)
        total = jnp.where(high, jnp.concatenate([other, total], axis=1), jnp.concatenate([total, other], axis=1))
    return total


def gram_total(values):
    return own_sum(local_gram(values))


def matmul(left, right):
    return jnp.einsum(
        "srt,stu->sru",
        left,
        right,
        precision=lax.Precision.HIGHEST,
        preferred_element_type=jnp.float32,
    )


def newton_turn(ortho, gram, eye, next_gram):
    square = matmul(gram, gram)
    poly = COEF_B * gram + COEF_C * square
    product = jnp.einsum(
        "srt,stk->srk",
        poly,
        ortho,
        precision=lax.Precision.HIGHEST,
        preferred_element_type=jnp.float32,
    )
    ortho = COEF_A * ortho + product
    if next_gram:
        step = COEF_A * eye + poly
        gram = matmul(step, matmul(gram, step))
    return ortho, gram


def on_device(partials, owner, momentum, master):
    group_count = lax.axis_size("x") * lax.axis_size("z")
    local_rows = partials[0]
    block_count = local_rows.shape[0]
    slot_count = momentum.shape[1]
    block_rows = momentum.shape[2]
    owner_list = owner[:, 0]
    target = slot_targets(owner_list, group_count, slot_count)
    present, source = slot_sources(target, group_count * slot_count, block_count)
    outgoing = jnp.where(present[:, None, None], jnp.take(local_rows, source, axis=0), 0)
    row_count = lax.axis_size("x")
    outgoing = outgoing.reshape((row_count, -1, slot_count) + outgoing.shape[1:])
    pieces = []
    for slot in range(slot_count):
        arrived = lax.all_to_all(outgoing[:, :, slot], "x", 0, 0, tiled=True)
        row_sum = jnp.sum(arrived.astype(jnp.float32), axis=0)
        pieces.append(lax.psum_scatter(row_sum, "z", scatter_dimension=0, tiled=True))
    gradient = jnp.concatenate(pieces, axis=0)
    momentum_new = BETA * momentum[0] + gradient
    update = gradient + BETA * momentum_new
    update_gram = gram_total(update)
    squares = jnp.trace(update_gram, axis1=1, axis2=2)
    factor = 1.0 / (jnp.sqrt(squares) + EPSILON)
    ortho = update * factor[:, None, None]
    gram = update_gram * (factor * factor)[:, None, None]
    eye = jnp.eye(block_rows, dtype=jnp.float32)[None]
    ortho, gram = lax.fori_loop(
        0, ITERS - 1, lambda _, carry: newton_turn(*carry, eye, True), (ortho, gram)
    )
    ortho, gram = newton_turn(ortho, gram, eye, False)
    step_factor = STEP_SIZE * 0.2 * math.sqrt(max(block_rows, D))
    master_new = master[0] * (1.0 - STEP_SIZE * DECAY) - step_factor * ortho
    weights_low = master_new.astype(jnp.bfloat16)
    every_slot = lax.all_gather(weights_low, ("x", "z"), axis=0, tiled=True)
    weights = jnp.take(every_slot, target, axis=0)
    return (momentum_new[None], master_new[None], weights)


def split_mesh(mesh):
    devices = mesh.devices
    row_count = len({device.coords[0] for device in devices[:, 0]})
    shape = (row_count, devices.shape[0] // row_count, devices.shape[1])
    return Mesh(devices.reshape(shape), ("x", "z", "own"))


def solution(mesh):
    grid = split_mesh(mesh)
    data = ("x", "z")
    in_specs = (
        P(data, None, None, "own"),
        P(),
        P(data, None, None, "own"),
        P(data, None, None, "own"),
    )
    out_specs = (P(data, None, None, "own"), P(data, None, None, "own"), P(None, None, "own"))
    return jax.shard_map(
        on_device, mesh=grid, in_specs=in_specs, out_specs=out_specs, check_vma=False
    )
```

```python
import math

import jax
import jax.numpy as jnp
from jax import lax
from jax.sharding import Mesh, PartitionSpec as P

D = 1024
ITERS = 5


COEF_A = 3.4445
COEF_B = -4.775
COEF_C = 2.0315
BETA = 0.95
STEP_SIZE = 0.2
DECAY = 0.1
EPSILON = 1e-07


def slot_targets(owner_list, group_count, slot_count):
    onehot = (owner_list[:, None] == jnp.arange(group_count, dtype=jnp.int32)[None, :]).astype(
        jnp.int32
    )
    before = jnp.cumsum(onehot, axis=0) - onehot
    ranks = jnp.sum(before * onehot, axis=1)
    return owner_list * slot_count + ranks


def slot_sources(target, slot_count, block_count):
    positions = jnp.arange(slot_count, dtype=jnp.int32)
    matches = positions[:, None] == target[None, :]
    present = jnp.any(matches, axis=1)
    source = jnp.sum(
        jnp.where(matches, jnp.arange(block_count, dtype=jnp.int32)[None, :], 0), axis=1
    )
    return (present, source)


def local_gram(values):
    return jnp.einsum(
        "srk,stk->srt",
        values,
        values,
        precision=lax.Precision.HIGHEST,
        preferred_element_type=jnp.float32,
    )


def own_sum(total):
    size = lax.axis_size("own")
    index = lax.axis_index("own")
    bits = []
    bit = 1
    while bit < size:
        bits.append(bit)
        bit *= 2
    for bit in bits:
        high = (index & bit) != 0
        half = total.shape[1] // 2
        lower, upper = total[:, :half], total[:, half:]
        keep = jnp.where(high, upper, lower)
        send = jnp.where(high, lower, upper)
        pairs = [(i, i ^ bit) for i in range(size)]
        total = keep + lax.ppermute(send, "own", pairs)
    for bit in reversed(bits):
        high = (index & bit) != 0
        pairs = [(i, i ^ bit) for i in range(size)]
        other = lax.ppermute(total, "own", pairs)
        total = jnp.where(high, jnp.concatenate([other, total], axis=1), jnp.concatenate([total, other], axis=1))
    return total


def gram_total(values):
    return own_sum(local_gram(values))


def matmul(left, right):
    return jnp.einsum(
        "srt,stu->sru",
        left,
        right,
        precision=lax.Precision.HIGHEST,
        preferred_element_type=jnp.float32,
    )


def newton_turn(ortho, gram, eye, next_gram):
    square = matmul(gram, gram)
    poly = COEF_B * gram + COEF_C * square
    product = jnp.einsum(
        "srt,stk->srk",
        poly,
        ortho,
        precision=lax.Precision.HIGHEST,
        preferred_element_type=jnp.float32,
    )
    ortho = COEF_A * ortho + product
    if next_gram:
        step = COEF_A * eye + poly
        gram = matmul(step, matmul(gram, step))
    return ortho, gram


def on_device(partials, owner, momentum, master):
    group_count = lax.axis_size("x") * lax.axis_size("z")
    local_rows = partials[0]
    block_count = local_rows.shape[0]
    slot_count = momentum.shape[1]
    block_rows = momentum.shape[2]
    owner_list = owner[:, 0]
    target = slot_targets(owner_list, group_count, slot_count)
    present, source = slot_sources(target, group_count * slot_count, block_count)
    outgoing = jnp.where(present[:, None, None], jnp.take(local_rows, source, axis=0, mode="clip"), 0)
    row_count = lax.axis_size("x")
    outgoing = outgoing.reshape((row_count, -1) + outgoing.shape[1:])
    arrived = lax.all_to_all(outgoing, "x", 0, 0, tiled=True)
    row_sum = jnp.sum(arrived.astype(jnp.float32), axis=0)
    gradient = lax.psum_scatter(row_sum, "z", scatter_dimension=0, tiled=True)
    momentum_new = BETA * momentum[0] + gradient
    update = gradient + BETA * momentum_new
    update_gram = gram_total(update)
    squares = jnp.trace(update_gram, axis1=1, axis2=2)
    factor = 1.0 / (jnp.sqrt(squares) + EPSILON)
    ortho = update * factor[:, None, None]
    gram = update_gram * (factor * factor)[:, None, None]
    eye = jnp.eye(block_rows, dtype=jnp.float32)[None]
    ortho, gram = lax.fori_loop(
        0, ITERS - 1, lambda _, carry: newton_turn(*carry, eye, True), (ortho, gram)
    )
    ortho, gram = newton_turn(ortho, gram, eye, False)
    step_factor = STEP_SIZE * 0.2 * math.sqrt(max(block_rows, D))
    master_new = master[0] * (1.0 - STEP_SIZE * DECAY) - step_factor * ortho
    weights_low = master_new.astype(jnp.bfloat16)
    column = lax.all_gather(weights_low, "z", axis=0, tiled=True)
    every_slot = lax.all_gather(column, "x", axis=0, tiled=True)
    weights = jnp.take(every_slot, target, axis=0, mode="clip")
    return (momentum_new[None], master_new[None], weights)


def split_mesh(mesh):
    devices = mesh.devices
    row_count = len({device.coords[0] for device in devices[:, 0]})
    shape = (row_count, devices.shape[0] // row_count, devices.shape[1])
    return Mesh(devices.reshape(shape), ("x", "z", "own"))


def solution(mesh):
    grid = split_mesh(mesh)
    data = ("x", "z")
    in_specs = (
        P(data, None, None, "own"),
        P(),
        P(data, None, None, "own"),
        P(data, None, None, "own"),
    )
    out_specs = (P(data, None, None, "own"), P(data, None, None, "own"), P(None, None, "own"))
    return jax.shard_map(
        on_device, mesh=grid, in_specs=in_specs, out_specs=out_specs, check_vma=False
    )
```

```python
import math

import jax
import jax.numpy as jnp
from jax import lax
from jax.sharding import Mesh, PartitionSpec as P

D = 1024
ITERS = 5


COEF_A = 3.4445
COEF_B = -4.775
COEF_C = 2.0315
BETA = 0.95
STEP_SIZE = 0.2
DECAY = 0.1
EPSILON = 1e-07


def slot_targets(owner_list, group_count, slot_count):
    onehot = (owner_list[:, None] == jnp.arange(group_count, dtype=jnp.int32)[None, :]).astype(
        jnp.int32
    )
    before = jnp.cumsum(onehot, axis=0) - onehot
    ranks = jnp.sum(before * onehot, axis=1)
    return owner_list * slot_count + ranks


def slot_sources(target, slot_count, block_count):
    positions = jnp.arange(slot_count, dtype=jnp.int32)
    matches = positions[:, None] == target[None, :]
    present = jnp.any(matches, axis=1)
    source = jnp.sum(
        jnp.where(matches, jnp.arange(block_count, dtype=jnp.int32)[None, :], 0), axis=1
    )
    return (present, source)


def local_gram(values):
    return jnp.einsum(
        "srk,stk->srt",
        values,
        values,
        precision=lax.Precision.HIGHEST,
        preferred_element_type=jnp.float32,
    )


def own_sum(total):
    size = lax.axis_size("own")
    index = lax.axis_index("own")
    rows = total.shape[1]
    core_pairs = [(i, i ^ 1) for i in range(size)]
    high = (index & 1) != 0
    lower, upper = total[:, : rows // 2], total[:, rows // 2 :]
    keep = jnp.where(high, upper, lower)
    total = keep + lax.ppermute(jnp.where(high, lower, upper), "own", core_pairs)
    chips = size // 2
    chip = index // 2
    piece = total.shape[1] // chips
    quarters = total.reshape(total.shape[0], chips, piece, total.shape[2])
    summed = jnp.take(quarters, chip, axis=1, mode="clip")
    for shift in range(1, chips):
        pairs = [(i, i ^ (2 * shift)) for i in range(size)]
        summed = summed + lax.ppermute(
            jnp.take(quarters, chip ^ shift, axis=1, mode="clip"), "own", pairs
        )
    arrived = [summed]
    for shift in range(1, chips):
        pairs = [(i, i ^ (2 * shift)) for i in range(size)]
        arrived.append(lax.ppermute(summed, "own", pairs))
    arrived = jnp.stack(arrived, axis=1)
    order = jnp.arange(chips, dtype=jnp.int32) ^ chip
    total = jnp.take(arrived, order, axis=1, mode="clip").reshape(total.shape)
    other = lax.ppermute(total, "own", core_pairs)
    return jnp.where(high, jnp.concatenate([other, total], axis=1), jnp.concatenate([total, other], axis=1))


def gram_total(values):
    return own_sum(local_gram(values))


def matmul(left, right):
    return jnp.einsum(
        "srt,stu->sru",
        left,
        right,
        precision=lax.Precision.HIGHEST,
        preferred_element_type=jnp.float32,
    )


def newton_turn(ortho, gram, eye, next_gram):
    square = matmul(gram, gram)
    poly = COEF_B * gram + COEF_C * square
    product = jnp.einsum(
        "srt,stk->srk",
        poly,
        ortho,
        precision=lax.Precision.HIGHEST,
        preferred_element_type=jnp.float32,
    )
    ortho = COEF_A * ortho + product
    if next_gram:
        step = COEF_A * eye + poly
        gram = matmul(step, matmul(gram, step))
    return ortho, gram


def on_device(partials, owner, momentum, master):
    group_count = lax.axis_size("x") * lax.axis_size("z")
    local_rows = partials[0]
    block_count = local_rows.shape[0]
    slot_count = momentum.shape[1]
    block_rows = momentum.shape[2]
    owner_list = owner[:, 0]
    target = slot_targets(owner_list, group_count, slot_count)
    present, source = slot_sources(target, group_count * slot_count, block_count)
    outgoing = jnp.where(present[:, None, None], jnp.take(local_rows, source, axis=0, mode="clip"), 0)
    row_count = lax.axis_size("x")
    outgoing = outgoing.reshape((row_count, -1) + outgoing.shape[1:])
    arrived = lax.all_to_all(outgoing, "x", 0, 0, tiled=True)
    row_sum = jnp.sum(arrived.astype(jnp.float32), axis=0)
    gradient = lax.psum_scatter(row_sum, "z", scatter_dimension=0, tiled=True)
    momentum_new = BETA * momentum[0] + gradient
    update = gradient + BETA * momentum_new
    update_gram = gram_total(update)
    squares = jnp.trace(update_gram, axis1=1, axis2=2)
    factor = 1.0 / (jnp.sqrt(squares) + EPSILON)
    ortho = update * factor[:, None, None]
    gram = update_gram * (factor * factor)[:, None, None]
    eye = jnp.eye(block_rows, dtype=jnp.float32)[None]
    ortho, gram = lax.fori_loop(
        0, ITERS - 1, lambda _, carry: newton_turn(*carry, eye, True), (ortho, gram)
    )
    ortho, gram = newton_turn(ortho, gram, eye, False)
    step_factor = STEP_SIZE * 0.2 * math.sqrt(max(block_rows, D))
    master_new = master[0] * (1.0 - STEP_SIZE * DECAY) - step_factor * ortho
    weights_low = master_new.astype(jnp.bfloat16)
    every_slot = lax.all_gather(weights_low, ("x", "z"), axis=0, tiled=True)
    weights = jnp.take(every_slot, target, axis=0, mode="clip")
    return (momentum_new[None], master_new[None], weights)


def split_mesh(mesh):
    devices = mesh.devices
    row_count = len({device.coords[0] for device in devices[:, 0]})
    shape = (row_count, devices.shape[0] // row_count, devices.shape[1])
    return Mesh(devices.reshape(shape), ("x", "z", "own"))


def solution(mesh):
    grid = split_mesh(mesh)
    data = ("x", "z")
    in_specs = (
        P(data, None, None, "own"),
        P(),
        P(data, None, None, "own"),
        P(data, None, None, "own"),
    )
    out_specs = (P(data, None, None, "own"), P(data, None, None, "own"), P(None, None, "own"))
    return jax.shard_map(
        on_device, mesh=grid, in_specs=in_specs, out_specs=out_specs, check_vma=False
    )
```

```python
import math

import jax
import jax.numpy as jnp
from jax import lax
from jax.sharding import Mesh, PartitionSpec as P

D = 1024
ITERS = 5


COEF_A = 3.4445
COEF_B = -4.775
COEF_C = 2.0315
BETA = 0.95
STEP_SIZE = 0.2
DECAY = 0.1
EPSILON = 1e-07


def slot_targets(owner_list, group_count, slot_count):
    onehot = (owner_list[:, None] == jnp.arange(group_count, dtype=jnp.int32)[None, :]).astype(
        jnp.int32
    )
    before = jnp.cumsum(onehot, axis=0) - onehot
    ranks = jnp.sum(before * onehot, axis=1)
    return owner_list * slot_count + ranks


def slot_sources(target, slot_count, block_count):
    positions = jnp.arange(slot_count, dtype=jnp.int32)
    matches = positions[:, None] == target[None, :]
    present = jnp.any(matches, axis=1)
    source = jnp.sum(
        jnp.where(matches, jnp.arange(block_count, dtype=jnp.int32)[None, :], 0), axis=1
    )
    return (present, source)


def local_gram(values):
    return jnp.einsum(
        "srk,stk->srt",
        values,
        values,
        precision=lax.Precision.HIGHEST,
        preferred_element_type=jnp.float32,
    )


def own_sum(total):
    size = lax.axis_size("own")
    index = lax.axis_index("own")
    rows = total.shape[1]
    core_pairs = [(i, i ^ 1) for i in range(size)]
    high = (index & 1) != 0
    lower, upper = total[:, : rows // 2], total[:, rows // 2 :]
    keep = jnp.where(high, upper, lower)
    total = keep + lax.ppermute(jnp.where(high, lower, upper), "own", core_pairs)
    chips = size // 2
    chip = index // 2
    piece = total.shape[1] // chips
    quarters = total.reshape(total.shape[0], chips, piece, total.shape[2])
    summed = jnp.take(quarters, chip, axis=1, mode="clip")
    for shift in range(1, chips):
        pairs = [(i, i ^ (2 * shift)) for i in range(size)]
        summed = summed + lax.ppermute(
            jnp.take(quarters, chip ^ shift, axis=1, mode="clip"), "own", pairs
        )
    arrived = [summed]
    for shift in range(1, chips):
        pairs = [(i, i ^ (2 * shift)) for i in range(size)]
        arrived.append(lax.ppermute(summed, "own", pairs))
    arrived = jnp.stack(arrived, axis=1)
    order = jnp.arange(chips, dtype=jnp.int32) ^ chip
    total = jnp.take(arrived, order, axis=1, mode="clip").reshape(total.shape)
    other = lax.ppermute(total, "own", core_pairs)
    return jnp.where(high, jnp.concatenate([other, total], axis=1), jnp.concatenate([total, other], axis=1))


def gram_total(values):
    return own_sum(local_gram(values))


def matmul(left, right):
    return jnp.einsum(
        "srt,stu->sru",
        left,
        right,
        precision=lax.Precision.HIGHEST,
        preferred_element_type=jnp.float32,
    )


def newton_turn(ortho, gram, eye, next_gram):
    square = matmul(gram, gram)
    poly = COEF_B * gram + COEF_C * square
    product = jnp.einsum(
        "srt,stk->srk",
        poly,
        ortho,
        precision=lax.Precision.HIGHEST,
        preferred_element_type=jnp.float32,
    )
    ortho = COEF_A * ortho + product
    if next_gram:
        step = COEF_A * eye + poly
        gram = matmul(step, matmul(gram, step))
    return ortho, gram


def on_device(partials, owner, momentum, master):
    group_count = lax.axis_size("x") * lax.axis_size("z")
    local_rows = partials[0]
    block_count = local_rows.shape[0]
    slot_count = momentum.shape[1]
    block_rows = momentum.shape[2]
    owner_list = owner[:, 0]
    target = slot_targets(owner_list, group_count, slot_count)
    present, source = slot_sources(target, group_count * slot_count, block_count)
    outgoing = jnp.take(local_rows, source, axis=0, mode="clip")
    row_count = lax.axis_size("x")
    outgoing = outgoing.reshape((row_count, -1) + outgoing.shape[1:])
    arrived = lax.all_to_all(outgoing, "x", 0, 0, tiled=True)
    row_present = jnp.take(present.reshape(row_count, -1), lax.axis_index("x"), axis=0, mode="clip")
    row_sum = jnp.where(row_present[:, None, None], jnp.sum(arrived.astype(jnp.float32), axis=0), 0.0)
    gradient = lax.psum_scatter(row_sum, "z", scatter_dimension=0, tiled=True)
    momentum_new = BETA * momentum[0] + gradient
    update = gradient + BETA * momentum_new
    update_gram = gram_total(update)
    squares = jnp.trace(update_gram, axis1=1, axis2=2)
    factor = 1.0 / (jnp.sqrt(squares) + EPSILON)
    ortho = update * factor[:, None, None]
    gram = update_gram * (factor * factor)[:, None, None]
    eye = jnp.eye(block_rows, dtype=jnp.float32)[None]
    ortho, gram = lax.fori_loop(
        0, ITERS - 1, lambda _, carry: newton_turn(*carry, eye, True), (ortho, gram)
    )
    ortho, gram = newton_turn(ortho, gram, eye, False)
    step_factor = STEP_SIZE * 0.2 * math.sqrt(max(block_rows, D))
    master_new = master[0] * (1.0 - STEP_SIZE * DECAY) - step_factor * ortho
    weights_low = master_new.astype(jnp.bfloat16)
    every_slot = lax.all_gather(weights_low, ("x", "z"), axis=0, tiled=True)
    weights = jnp.take(every_slot, target, axis=0, mode="clip")
    return (momentum_new[None], master_new[None], weights)


def split_mesh(mesh):
    devices = mesh.devices
    row_count = len({device.coords[0] for device in devices[:, 0]})
    shape = (row_count, devices.shape[0] // row_count, devices.shape[1])
    return Mesh(devices.reshape(shape), ("x", "z", "own"))


def solution(mesh):
    grid = split_mesh(mesh)
    data = ("x", "z")
    in_specs = (
        P(data, None, None, "own"),
        P(),
        P(data, None, None, "own"),
        P(data, None, None, "own"),
    )
    out_specs = (P(data, None, None, "own"), P(data, None, None, "own"), P(None, None, "own"))
    return jax.shard_map(
        on_device, mesh=grid, in_specs=in_specs, out_specs=out_specs, check_vma=False
    )
```

```python
import math

import jax
import jax.numpy as jnp
from jax import lax
from jax.sharding import Mesh, PartitionSpec as P

D = 1024
ITERS = 5


COEF_A = 3.4445
COEF_B = -4.775
COEF_C = 2.0315
BETA = 0.95
STEP_SIZE = 0.2
DECAY = 0.1
EPSILON = 1e-07


def slot_targets(owner_list, group_count, slot_count):
    onehot = (owner_list[:, None] == jnp.arange(group_count, dtype=jnp.int32)[None, :]).astype(
        jnp.int32
    )
    before = jnp.cumsum(onehot, axis=0) - onehot
    ranks = jnp.sum(before * onehot, axis=1)
    return owner_list * slot_count + ranks


def slot_sources(target, slot_count, block_count):
    positions = jnp.arange(slot_count, dtype=jnp.int32)
    matches = positions[:, None] == target[None, :]
    present = jnp.any(matches, axis=1)
    source = jnp.sum(
        jnp.where(matches, jnp.arange(block_count, dtype=jnp.int32)[None, :], 0), axis=1
    )
    return (present, source)


def local_gram(values):
    return jnp.einsum(
        "srk,stk->srt",
        values,
        values,
        precision=lax.Precision.HIGHEST,
        preferred_element_type=jnp.float32,
    )


def own_sum(total):
    size = lax.axis_size("own")
    index = lax.axis_index("own")
    rows = total.shape[1]
    core_pairs = [(i, i ^ 1) for i in range(size)]
    high = (index & 1) != 0
    lower, upper = total[:, : rows // 2], total[:, rows // 2 :]
    keep = jnp.where(high, upper, lower)
    total = keep + lax.ppermute(jnp.where(high, lower, upper), "own", core_pairs)
    chips = size // 2
    chip = index // 2
    piece = total.shape[1] // chips
    quarters = total.reshape(total.shape[0], chips, piece, total.shape[2])
    summed = jnp.take(quarters, chip, axis=1, mode="clip")
    for shift in range(1, chips):
        pairs = [(i, i ^ (2 * shift)) for i in range(size)]
        summed = summed + lax.ppermute(
            jnp.take(quarters, chip ^ shift, axis=1, mode="clip"), "own", pairs
        )
    arrived = [summed]
    for shift in range(1, chips):
        pairs = [(i, i ^ (2 * shift)) for i in range(size)]
        arrived.append(lax.ppermute(summed, "own", pairs))
    arrived = jnp.stack(arrived, axis=1)
    order = jnp.arange(chips, dtype=jnp.int32) ^ chip
    total = jnp.take(arrived, order, axis=1, mode="clip").reshape(total.shape)
    other = lax.ppermute(total, "own", core_pairs)
    return jnp.where(high, jnp.concatenate([other, total], axis=1), jnp.concatenate([total, other], axis=1))


def gram_total(values):
    return own_sum(local_gram(values))


def matmul(left, right):
    return jnp.einsum(
        "srt,stu->sru",
        left,
        right,
        precision=lax.Precision.HIGHEST,
        preferred_element_type=jnp.float32,
    )


def newton_turn(ortho, gram, eye, next_gram):
    square = matmul(gram, gram)
    poly = COEF_B * gram + COEF_C * square
    product = jnp.einsum(
        "srt,stk->srk",
        poly,
        ortho,
        precision=lax.Precision.HIGHEST,
        preferred_element_type=jnp.float32,
    )
    ortho = COEF_A * ortho + product
    if next_gram:
        step = COEF_A * eye + poly
        gram = matmul(step, matmul(gram, step))
    return ortho, gram


def on_device(partials, owner, momentum, master):
    group_count = lax.axis_size("x") * lax.axis_size("z")
    local_rows = partials[0]
    block_count = local_rows.shape[0]
    slot_count = momentum.shape[1]
    block_rows = momentum.shape[2]
    owner_list = owner[:, 0]
    target = slot_targets(owner_list, group_count, slot_count)
    present, source = slot_sources(target, group_count * slot_count, block_count)
    row_count = lax.axis_size("x")
    row_slots = group_count * slot_count // row_count
    width = row_slots * 3 // 4
    row_of = target // row_slots
    row_hot = (row_of[:, None] == jnp.arange(row_count, dtype=jnp.int32)[None, :]).astype(jnp.int32)
    row_rank = jnp.sum((jnp.cumsum(row_hot, axis=0) - row_hot) * row_hot, axis=1)
    fits = jnp.max(jnp.sum(row_hot, axis=0)) <= width
    here = lax.axis_index("x")
    row_present = jnp.take(present.reshape(row_count, -1), here, axis=0, mode="clip")

    def padded(rows):
        outgoing = jnp.take(rows, source, axis=0, mode="clip")
        outgoing = outgoing.reshape((row_count, -1) + outgoing.shape[1:])
        arrived = lax.all_to_all(outgoing, "x", 0, 0, tiled=True)
        return jnp.where(row_present[:, None, None], jnp.sum(arrived.astype(jnp.float32), axis=0), 0.0)

    def packed(rows):
        spot = row_of * width + row_rank
        hits = jnp.arange(row_count * width, dtype=jnp.int32)[:, None] == spot[None, :]
        send_index = jnp.sum(jnp.where(hits, jnp.arange(block_count, dtype=jnp.int32)[None, :], 0), axis=1)
        outgoing = jnp.take(rows, send_index, axis=0, mode="clip")
        outgoing = outgoing.reshape((row_count, width) + outgoing.shape[1:])
        arrived = lax.all_to_all(outgoing, "x", 0, 0, tiled=True)
        packed_sum = jnp.sum(arrived.astype(jnp.float32), axis=0)
        slots_here = here * row_slots + jnp.arange(row_slots, dtype=jnp.int32)
        owners = slots_here[:, None] == target[None, :]
        receive_index = jnp.sum(jnp.where(owners, row_rank[None, :], 0), axis=1)
        placed = jnp.take(packed_sum, receive_index, axis=0, mode="clip")
        return jnp.where(row_present[:, None, None], placed, 0.0)

    row_sum = lax.cond(fits, packed, padded, local_rows)
    gradient = lax.psum_scatter(row_sum, "z", scatter_dimension=0, tiled=True)
    momentum_new = BETA * momentum[0] + gradient
    update = gradient + BETA * momentum_new
    update_gram = gram_total(update)
    squares = jnp.trace(update_gram, axis1=1, axis2=2)
    factor = 1.0 / (jnp.sqrt(squares) + EPSILON)
    ortho = update * factor[:, None, None]
    gram = update_gram * (factor * factor)[:, None, None]
    eye = jnp.eye(block_rows, dtype=jnp.float32)[None]
    ortho, gram = lax.fori_loop(
        0, ITERS - 1, lambda _, carry: newton_turn(*carry, eye, True), (ortho, gram)
    )
    ortho, gram = newton_turn(ortho, gram, eye, False)
    step_factor = STEP_SIZE * 0.2 * math.sqrt(max(block_rows, D))
    master_new = master[0] * (1.0 - STEP_SIZE * DECAY) - step_factor * ortho
    weights_low = master_new.astype(jnp.bfloat16)
    every_slot = lax.all_gather(weights_low, ("x", "z"), axis=0, tiled=True)
    weights = jnp.take(every_slot, target, axis=0, mode="clip")
    return (momentum_new[None], master_new[None], weights)


def split_mesh(mesh):
    devices = mesh.devices
    row_count = len({device.coords[0] for device in devices[:, 0]})
    shape = (row_count, devices.shape[0] // row_count, devices.shape[1])
    return Mesh(devices.reshape(shape), ("x", "z", "own"))


def solution(mesh):
    grid = split_mesh(mesh)
    data = ("x", "z")
    in_specs = (
        P(data, None, None, "own"),
        P(),
        P(data, None, None, "own"),
        P(data, None, None, "own"),
    )
    out_specs = (P(data, None, None, "own"), P(data, None, None, "own"), P(None, None, "own"))
    return jax.shard_map(
        on_device, mesh=grid, in_specs=in_specs, out_specs=out_specs, check_vma=False
    )
```

```python
import math

import jax
import jax.numpy as jnp
from jax import lax
from jax.sharding import Mesh, PartitionSpec as P

D = 1024
ITERS = 5


COEF_A = 3.4445
COEF_B = -4.775
COEF_C = 2.0315
BETA = 0.95
STEP_SIZE = 0.2
DECAY = 0.1
EPSILON = 1e-07


def slot_targets(owner_list, group_count, slot_count):
    onehot = (owner_list[:, None] == jnp.arange(group_count, dtype=jnp.int32)[None, :]).astype(
        jnp.int32
    )
    before = jnp.cumsum(onehot, axis=0) - onehot
    ranks = jnp.sum(before * onehot, axis=1)
    return owner_list * slot_count + ranks


def slot_sources(target, slot_count, block_count):
    positions = jnp.arange(slot_count, dtype=jnp.int32)
    matches = positions[:, None] == target[None, :]
    present = jnp.any(matches, axis=1)
    source = jnp.sum(
        jnp.where(matches, jnp.arange(block_count, dtype=jnp.int32)[None, :], 0), axis=1
    )
    return (present, source)


def local_gram(values):
    return jnp.einsum(
        "srk,stk->srt",
        values,
        values,
        precision=lax.Precision.HIGHEST,
        preferred_element_type=jnp.float32,
    )


def own_sum(total):
    size = lax.axis_size("own")
    index = lax.axis_index("own")
    rows = total.shape[1]
    core_pairs = [(i, i ^ 1) for i in range(size)]
    high = (index & 1) != 0
    lower, upper = total[:, : rows // 2], total[:, rows // 2 :]
    keep = jnp.where(high, upper, lower)
    total = keep + lax.ppermute(jnp.where(high, lower, upper), "own", core_pairs)
    chips = size // 2
    chip = index // 2
    piece = total.shape[1] // chips
    quarters = total.reshape(total.shape[0], chips, piece, total.shape[2])
    summed = jnp.take(quarters, chip, axis=1, mode="clip")
    for shift in range(1, chips):
        pairs = [(i, i ^ (2 * shift)) for i in range(size)]
        summed = summed + lax.ppermute(
            jnp.take(quarters, chip ^ shift, axis=1, mode="clip"), "own", pairs
        )
    arrived = [summed]
    for shift in range(1, chips):
        pairs = [(i, i ^ (2 * shift)) for i in range(size)]
        arrived.append(lax.ppermute(summed, "own", pairs))
    arrived = jnp.stack(arrived, axis=1)
    order = jnp.arange(chips, dtype=jnp.int32) ^ chip
    total = jnp.take(arrived, order, axis=1, mode="clip").reshape(total.shape)
    other = lax.ppermute(total, "own", core_pairs)
    return jnp.where(high, jnp.concatenate([other, total], axis=1), jnp.concatenate([total, other], axis=1))


def gram_total(values):
    return own_sum(local_gram(values))


def matmul(left, right):
    return jnp.einsum(
        "srt,stu->sru",
        left,
        right,
        precision=lax.Precision.HIGHEST,
        preferred_element_type=jnp.float32,
    )


def newton_turn(ortho, gram, eye, next_gram):
    square = matmul(gram, gram)
    poly = COEF_B * gram + COEF_C * square
    product = jnp.einsum(
        "srt,stk->srk",
        poly,
        ortho,
        precision=lax.Precision.HIGHEST,
        preferred_element_type=jnp.float32,
    )
    ortho = COEF_A * ortho + product
    if next_gram:
        step = COEF_A * eye + poly
        gram = matmul(step, matmul(gram, step))
    return ortho, gram


def on_device(partials, owner, momentum, master):
    group_count = lax.axis_size("x") * lax.axis_size("z")
    local_rows = partials[0]
    block_count = local_rows.shape[0]
    slot_count = momentum.shape[1]
    block_rows = momentum.shape[2]
    owner_list = owner[:, 0]
    target = slot_targets(owner_list, group_count, slot_count)
    present, source = slot_sources(target, group_count * slot_count, block_count)
    row_count = lax.axis_size("x")
    row_slots = group_count * slot_count // row_count
    width = row_slots * 3 // 4
    row_of = target // row_slots
    row_hot = (row_of[:, None] == jnp.arange(row_count, dtype=jnp.int32)[None, :]).astype(jnp.int32)
    row_rank = jnp.sum((jnp.cumsum(row_hot, axis=0) - row_hot) * row_hot, axis=1)
    fits = jnp.max(jnp.sum(row_hot, axis=0)) <= width
    here = lax.axis_index("x")
    row_present = jnp.take(present.reshape(row_count, -1), here, axis=0, mode="clip")

    def padded(rows):
        outgoing = jnp.take(rows, source, axis=0, mode="clip")
        outgoing = outgoing.reshape((row_count, -1) + outgoing.shape[1:])
        arrived = lax.all_to_all(outgoing, "x", 0, 0, tiled=True)
        return jnp.where(row_present[:, None, None], jnp.sum(arrived.astype(jnp.float32), axis=0), 0.0)

    def packed(rows):
        spot = row_of * width + row_rank
        hits = jnp.arange(row_count * width, dtype=jnp.int32)[:, None] == spot[None, :]
        send_index = jnp.sum(jnp.where(hits, jnp.arange(block_count, dtype=jnp.int32)[None, :], 0), axis=1)
        outgoing = jnp.take(rows, send_index, axis=0, mode="clip")
        outgoing = outgoing.reshape((row_count, width) + outgoing.shape[1:])
        arrived = lax.all_to_all(outgoing, "x", 0, 0, tiled=True)
        packed_sum = jnp.sum(arrived.astype(jnp.float32), axis=0)
        packed_sum = jnp.concatenate([packed_sum, jnp.zeros_like(packed_sum[:1])], axis=0)
        slots_here = here * row_slots + jnp.arange(row_slots, dtype=jnp.int32)
        owners = slots_here[:, None] == target[None, :]
        receive_index = jnp.sum(jnp.where(owners, row_rank[None, :], 0), axis=1)
        receive_index = jnp.where(row_present, receive_index, width)
        return jnp.take(packed_sum, receive_index, axis=0, mode="clip")

    row_sum = lax.cond(fits, packed, padded, local_rows)
    gradient = lax.psum_scatter(row_sum, "z", scatter_dimension=0, tiled=True)
    momentum_new = BETA * momentum[0] + gradient
    update = gradient + BETA * momentum_new
    update_gram = gram_total(update)
    squares = jnp.trace(update_gram, axis1=1, axis2=2)
    factor = 1.0 / (jnp.sqrt(squares) + EPSILON)
    ortho = update * factor[:, None, None]
    gram = update_gram * (factor * factor)[:, None, None]
    eye = jnp.eye(block_rows, dtype=jnp.float32)[None]
    ortho, gram = lax.fori_loop(
        0, ITERS - 1, lambda _, carry: newton_turn(*carry, eye, True), (ortho, gram)
    )
    ortho, gram = newton_turn(ortho, gram, eye, False)
    step_factor = STEP_SIZE * 0.2 * math.sqrt(max(block_rows, D))
    master_new = master[0] * (1.0 - STEP_SIZE * DECAY) - step_factor * ortho
    weights_low = master_new.astype(jnp.bfloat16)
    every_slot = lax.all_gather(weights_low, ("x", "z"), axis=0, tiled=True)
    weights = jnp.take(every_slot, target, axis=0, mode="clip")
    return (momentum_new[None], master_new[None], weights)


def split_mesh(mesh):
    devices = mesh.devices
    row_count = len({device.coords[0] for device in devices[:, 0]})
    shape = (row_count, devices.shape[0] // row_count, devices.shape[1])
    return Mesh(devices.reshape(shape), ("x", "z", "own"))


def solution(mesh):
    grid = split_mesh(mesh)
    data = ("x", "z")
    in_specs = (
        P(data, None, None, "own"),
        P(),
        P(data, None, None, "own"),
        P(data, None, None, "own"),
    )
    out_specs = (P(data, None, None, "own"), P(data, None, None, "own"), P(None, None, "own"))
    return jax.shard_map(
        on_device, mesh=grid, in_specs=in_specs, out_specs=out_specs, check_vma=False
    )
```

```python
import math

import jax
import jax.numpy as jnp
from jax import lax
from jax.sharding import Mesh, PartitionSpec as P

D = 1024
ITERS = 5


COEF_A = 3.4445
COEF_B = -4.775
COEF_C = 2.0315
BETA = 0.95
STEP_SIZE = 0.2
DECAY = 0.1
EPSILON = 1e-07


def slot_targets(owner_list, group_count, slot_count):
    onehot = (owner_list[:, None] == jnp.arange(group_count, dtype=jnp.int32)[None, :]).astype(
        jnp.int32
    )
    before = jnp.cumsum(onehot, axis=0) - onehot
    ranks = jnp.sum(before * onehot, axis=1)
    return owner_list * slot_count + ranks


def slot_sources(target, slot_count, block_count):
    positions = jnp.arange(slot_count, dtype=jnp.int32)
    matches = positions[:, None] == target[None, :]
    present = jnp.any(matches, axis=1)
    source = jnp.sum(
        jnp.where(matches, jnp.arange(block_count, dtype=jnp.int32)[None, :], 0), axis=1
    )
    return (present, source)


def local_gram(values):
    return jnp.einsum(
        "srk,stk->srt",
        values,
        values,
        precision=lax.Precision.HIGHEST,
        preferred_element_type=jnp.float32,
    )


def own_sum(total):
    size = lax.axis_size("own")
    index = lax.axis_index("own")
    rows = total.shape[1]
    core_pairs = [(i, i ^ 1) for i in range(size)]
    high = (index & 1) != 0
    lower, upper = total[:, : rows // 2], total[:, rows // 2 :]
    keep = jnp.where(high, upper, lower)
    total = keep + lax.ppermute(jnp.where(high, lower, upper), "own", core_pairs)
    chips = size // 2
    chip = index // 2
    piece = total.shape[1] // chips
    quarters = total.reshape(total.shape[0], chips, piece, total.shape[2])
    summed = jnp.take(quarters, chip, axis=1, mode="clip")
    for shift in range(1, chips):
        pairs = [(i, i ^ (2 * shift)) for i in range(size)]
        summed = summed + lax.ppermute(
            jnp.take(quarters, chip ^ shift, axis=1, mode="clip"), "own", pairs
        )
    arrived = [summed]
    for shift in range(1, chips):
        pairs = [(i, i ^ (2 * shift)) for i in range(size)]
        arrived.append(lax.ppermute(summed, "own", pairs))
    arrived = jnp.stack(arrived, axis=1)
    order = jnp.arange(chips, dtype=jnp.int32) ^ chip
    total = jnp.take(arrived, order, axis=1, mode="clip").reshape(total.shape)
    other = lax.ppermute(total, "own", core_pairs)
    return jnp.where(high, jnp.concatenate([other, total], axis=1), jnp.concatenate([total, other], axis=1))


def gram_total(values):
    return own_sum(local_gram(values))


def matmul(left, right):
    return jnp.einsum(
        "srt,stu->sru",
        left,
        right,
        precision=lax.Precision.HIGHEST,
        preferred_element_type=jnp.float32,
    )


def newton_turn(ortho, gram, eye, next_gram):
    square = matmul(gram, gram)
    step = COEF_A * eye + COEF_B * gram + COEF_C * square
    if not next_gram:
        return matmul(step, ortho), gram
    width = ortho.shape[2]
    both = matmul(step, jnp.concatenate([ortho, matmul(gram, step)], axis=2))
    return both[:, :, :width], both[:, :, width:]


def own_sum(total):
    size = lax.axis_size("own")
    index = lax.axis_index("own")
    rows = total.shape[1]
    core_pairs = [(i, i ^ 1) for i in range(size)]
    high = (index & 1) != 0
    lower, upper = total[:, : rows // 2], total[:, rows // 2 :]
    keep = jnp.where(high, upper, lower)
    total = keep + lax.ppermute(jnp.where(high, lower, upper), "own", core_pairs)
    chips = size // 2
    chip = index // 2
    piece = total.shape[1] // chips
    quarters = total.reshape(total.shape[0], chips, piece, total.shape[2])
    summed = jnp.take(quarters, chip, axis=1, mode="clip")
    for shift in range(1, chips):
        pairs = [(i, i ^ (2 * shift)) for i in range(size)]
        summed = summed + lax.ppermute(
            jnp.take(quarters, chip ^ shift, axis=1, mode="clip"), "own", pairs
        )
    arrived = [summed]
    for shift in range(1, chips):
        pairs = [(i, i ^ (2 * shift)) for i in range(size)]
        arrived.append(lax.ppermute(summed, "own", pairs))
    arrived = jnp.stack(arrived, axis=1)
    order = jnp.arange(chips, dtype=jnp.int32) ^ chip
    total = jnp.take(arrived, order, axis=1, mode="clip").reshape(total.shape)
    other = lax.ppermute(total, "own", core_pairs)
    return jnp.where(high, jnp.concatenate([other, total], axis=1), jnp.concatenate([total, other], axis=1))


def gram_total(values):
    return own_sum(local_gram(values))


def matmul(left, right):
    return jnp.einsum(
        "srt,stu->sru",
        left,
        right,
        precision=lax.Precision.HIGHEST,
        preferred_element_type=jnp.float32,
    )


def newton_turn(ortho, gram, eye, next_gram):
    square = matmul(gram, gram)
    poly = COEF_B * gram + COEF_C * square
    product = jnp.einsum(
        "srt,stk->srk",
        poly,
        ortho,
        precision=lax.Precision.HIGHEST,
        preferred_element_type=jnp.float32,
    )
    ortho = COEF_A * ortho + product
    if next_gram:
        step = COEF_A * eye + poly
        gram = matmul(step, matmul(gram, step))
    return ortho, gram


def on_device(partials, owner, momentum, master):
    group_count = lax.axis_size("x") * lax.axis_size("z")
    local_rows = partials[0]
    block_count = local_rows.shape[0]
    slot_count = momentum.shape[1]
    block_rows = momentum.shape[2]
    owner_list = owner[:, 0]
    target = slot_targets(owner_list, group_count, slot_count)
    present, source = slot_sources(target, group_count * slot_count, block_count)
    row_count = lax.axis_size("x")
    row_slots = group_count * slot_count // row_count
    width = row_slots * 3 // 4
    row_of = target // row_slots
    row_hot = (row_of[:, None] == jnp.arange(row_count, dtype=jnp.int32)[None, :]).astype(jnp.int32)
    row_rank = jnp.sum((jnp.cumsum(row_hot, axis=0) - row_hot) * row_hot, axis=1)
    fits = jnp.max(jnp.sum(row_hot, axis=0)) <= width
    here = lax.axis_index("x")
    row_present = jnp.take(present.reshape(row_count, -1), here, axis=0, mode="clip")

    def padded(rows):
        outgoing = jnp.take(rows, source, axis=0, mode="clip")
        outgoing = outgoing.reshape((row_count, -1) + outgoing.shape[1:])
        arrived = lax.all_to_all(outgoing, "x", 0, 0, tiled=True)
        return jnp.where(row_present[:, None, None], jnp.sum(arrived.astype(jnp.float32), axis=0), 0.0)

    def packed(rows):
        spot = row_of * width + row_rank
        hits = jnp.arange(row_count * width, dtype=jnp.int32)[:, None] == spot[None, :]
        send_index = jnp.sum(jnp.where(hits, jnp.arange(block_count, dtype=jnp.int32)[None, :], 0), axis=1)
        outgoing = jnp.take(rows, send_index, axis=0, mode="clip")
        outgoing = outgoing.reshape((row_count, width) + outgoing.shape[1:])
        arrived = lax.all_to_all(outgoing, "x", 0, 0, tiled=True)
        packed_sum = jnp.sum(arrived.astype(jnp.float32), axis=0)
        packed_sum = jnp.concatenate([packed_sum, jnp.zeros_like(packed_sum[:1])], axis=0)
        slots_here = here * row_slots + jnp.arange(row_slots, dtype=jnp.int32)
        owners = slots_here[:, None] == target[None, :]
        receive_index = jnp.sum(jnp.where(owners, row_rank[None, :], 0), axis=1)
        receive_index = jnp.where(row_present, receive_index, width)
        return jnp.take(packed_sum, receive_index, axis=0, mode="clip")

    row_sum = lax.cond(fits, packed, padded, local_rows)
    gradient = lax.psum_scatter(row_sum, "z", scatter_dimension=0, tiled=True)
    momentum_new = BETA * momentum[0] + gradient
    update = gradient + BETA * momentum_new
    update_gram = gram_total(update)
    squares = jnp.trace(update_gram, axis1=1, axis2=2)
    factor = 1.0 / (jnp.sqrt(squares) + EPSILON)
    ortho = update * factor[:, None, None]
    gram = update_gram * (factor * factor)[:, None, None]
    eye = jnp.eye(block_rows, dtype=jnp.float32)[None]
    ortho, gram = lax.fori_loop(
        0, ITERS - 1, lambda _, carry: newton_turn(*carry, eye, True), (ortho, gram)
    )
    ortho, gram = newton_turn(ortho, gram, eye, False)
    step_factor = STEP_SIZE * 0.2 * math.sqrt(max(block_rows, D))
    master_new = master[0] * (1.0 - STEP_SIZE * DECAY) - step_factor * ortho
    weights_low = master_new.astype(jnp.bfloat16)
    every_slot = lax.all_gather(weights_low, ("x", "z"), axis=0, tiled=True)
    weights = jnp.take(every_slot, target, axis=0, mode="clip")
    return (momentum_new[None], master_new[None], weights)


def split_mesh(mesh):
    devices = mesh.devices
    row_count = len({device.coords[0] for device in devices[:, 0]})
    shape = (row_count, devices.shape[0] // row_count, devices.shape[1])
    return Mesh(devices.reshape(shape), ("x", "z", "own"))


def solution(mesh):
    grid = split_mesh(mesh)
    data = ("x", "z")
    in_specs = (
        P(data, None, None, "own"),
        P(),
        P(data, None, None, "own"),
        P(data, None, None, "own"),
    )
    out_specs = (P(data, None, None, "own"), P(data, None, None, "own"), P(None, None, "own"))
    return jax.shard_map(
        on_device, mesh=grid, in_specs=in_specs, out_specs=out_specs, check_vma=False
    )
```

```python
import math

import jax
import jax.numpy as jnp
from jax import lax
from jax.sharding import Mesh, PartitionSpec as P

D = 1024
ITERS = 5


COEF_A = 3.4445
COEF_B = -4.775
COEF_C = 2.0315
BETA = 0.95
STEP_SIZE = 0.2
DECAY = 0.1
EPSILON = 1e-07


def slot_targets(owner_list, group_count, slot_count):
    onehot = (owner_list[:, None] == jnp.arange(group_count, dtype=jnp.int32)[None, :]).astype(
        jnp.int32
    )
    before = jnp.cumsum(onehot, axis=0) - onehot
    ranks = jnp.sum(before * onehot, axis=1)
    return owner_list * slot_count + ranks


def slot_sources(target, slot_count, block_count):
    positions = jnp.arange(slot_count, dtype=jnp.int32)
    matches = positions[:, None] == target[None, :]
    present = jnp.any(matches, axis=1)
    source = jnp.sum(
        jnp.where(matches, jnp.arange(block_count, dtype=jnp.int32)[None, :], 0), axis=1
    )
    return (present, source)


def local_gram(values):
    return jnp.einsum(
        "srk,stk->srt",
        values,
        values,
        precision=lax.Precision.HIGHEST,
        preferred_element_type=jnp.float32,
    )


def own_sum(total):
    size = lax.axis_size("own")
    index = lax.axis_index("own")
    rows = total.shape[1]
    core_pairs = [(i, i ^ 1) for i in range(size)]
    high = (index & 1) != 0
    lower, upper = total[:, : rows // 2], total[:, rows // 2 :]
    keep = jnp.where(high, upper, lower)
    total = keep + lax.ppermute(jnp.where(high, lower, upper), "own", core_pairs)
    chips = size // 2
    chip = index // 2
    piece = total.shape[1] // chips
    quarters = total.reshape(total.shape[0], chips, piece, total.shape[2])
    summed = jnp.take(quarters, chip, axis=1, mode="clip")
    for shift in range(1, chips):
        pairs = [(i, i ^ (2 * shift)) for i in range(size)]
        summed = summed + lax.ppermute(
            jnp.take(quarters, chip ^ shift, axis=1, mode="clip"), "own", pairs
        )
    arrived = [summed]
    for shift in range(1, chips):
        pairs = [(i, i ^ (2 * shift)) for i in range(size)]
        arrived.append(lax.ppermute(summed, "own", pairs))
    arrived = jnp.stack(arrived, axis=1)
    order = jnp.arange(chips, dtype=jnp.int32) ^ chip
    total = jnp.take(arrived, order, axis=1, mode="clip").reshape(total.shape)
    other = lax.ppermute(total, "own", core_pairs)
    return jnp.where(high, jnp.concatenate([other, total], axis=1), jnp.concatenate([total, other], axis=1))


def gram_total(values):
    return own_sum(local_gram(values))


def matmul(left, right):
    return jnp.einsum(
        "srt,stu->sru",
        left,
        right,
        precision=lax.Precision.HIGHEST,
        preferred_element_type=jnp.float32,
    )


def newton_turn(ortho, gram, eye, next_gram):
    square = matmul(gram, gram)
    poly = COEF_B * gram + COEF_C * square
    product = jnp.einsum(
        "srt,stk->srk",
        poly,
        ortho,
        precision=lax.Precision.HIGHEST,
        preferred_element_type=jnp.float32,
    )
    ortho = COEF_A * ortho + product
    if next_gram:
        step = COEF_A * eye + poly
        gram = matmul(step, matmul(gram, step))
    return ortho, gram


def on_device(partials, owner, momentum, master):
    group_count = lax.axis_size("x") * lax.axis_size("z")
    local_rows = partials[0]
    block_count = local_rows.shape[0]
    slot_count = momentum.shape[1]
    block_rows = momentum.shape[2]
    owner_list = owner[:, 0]
    target = slot_targets(owner_list, group_count, slot_count)
    present, source = slot_sources(target, group_count * slot_count, block_count)
    row_count = lax.axis_size("x")
    row_slots = group_count * slot_count // row_count
    width = row_slots * 11 // 16
    row_of = target // row_slots
    row_hot = (row_of[:, None] == jnp.arange(row_count, dtype=jnp.int32)[None, :]).astype(jnp.int32)
    row_rank = jnp.sum((jnp.cumsum(row_hot, axis=0) - row_hot) * row_hot, axis=1)
    fits = jnp.max(jnp.sum(row_hot, axis=0)) <= width
    here = lax.axis_index("x")
    row_present = jnp.take(present.reshape(row_count, -1), here, axis=0, mode="clip")

    def padded(rows):
        outgoing = jnp.take(rows, source, axis=0, mode="clip")
        outgoing = outgoing.reshape((row_count, -1) + outgoing.shape[1:])
        arrived = lax.all_to_all(outgoing, "x", 0, 0, tiled=True)
        return jnp.where(row_present[:, None, None], jnp.sum(arrived.astype(jnp.float32), axis=0), 0.0)

    def packed(rows):
        spot = row_of * width + row_rank
        hits = jnp.arange(row_count * width, dtype=jnp.int32)[:, None] == spot[None, :]
        send_index = jnp.sum(jnp.where(hits, jnp.arange(block_count, dtype=jnp.int32)[None, :], 0), axis=1)
        outgoing = jnp.take(rows, send_index, axis=0, mode="clip")
        outgoing = outgoing.reshape((row_count, width) + outgoing.shape[1:])
        arrived = lax.all_to_all(outgoing, "x", 0, 0, tiled=True)
        packed_sum = jnp.sum(arrived.astype(jnp.float32), axis=0)
        packed_sum = jnp.concatenate([packed_sum, jnp.zeros_like(packed_sum[:1])], axis=0)
        slots_here = here * row_slots + jnp.arange(row_slots, dtype=jnp.int32)
        owners = slots_here[:, None] == target[None, :]
        receive_index = jnp.sum(jnp.where(owners, row_rank[None, :], 0), axis=1)
        receive_index = jnp.where(row_present, receive_index, width)
        return jnp.take(packed_sum, receive_index, axis=0, mode="clip")

    row_sum = lax.cond(fits, packed, padded, local_rows)
    gradient = lax.psum_scatter(row_sum, "z", scatter_dimension=0, tiled=True)
    momentum_new = BETA * momentum[0] + gradient
    update = gradient + BETA * momentum_new
    update_gram = gram_total(update)
    squares = jnp.trace(update_gram, axis1=1, axis2=2)
    factor = 1.0 / (jnp.sqrt(squares) + EPSILON)
    ortho = update * factor[:, None, None]
    gram = update_gram * (factor * factor)[:, None, None]
    eye = jnp.eye(block_rows, dtype=jnp.float32)[None]
    ortho, gram = lax.fori_loop(
        0, ITERS - 1, lambda _, carry: newton_turn(*carry, eye, True), (ortho, gram)
    )
    ortho, gram = newton_turn(ortho, gram, eye, False)
    step_factor = STEP_SIZE * 0.2 * math.sqrt(max(block_rows, D))
    master_new = master[0] * (1.0 - STEP_SIZE * DECAY) - step_factor * ortho
    weights_low = master_new.astype(jnp.bfloat16)
    every_slot = lax.all_gather(weights_low, ("x", "z"), axis=0, tiled=True)
    weights = jnp.take(every_slot, target, axis=0, mode="clip")
    return (momentum_new[None], master_new[None], weights)


def split_mesh(mesh):
    devices = mesh.devices
    row_count = len({device.coords[0] for device in devices[:, 0]})
    shape = (row_count, devices.shape[0] // row_count, devices.shape[1])
    return Mesh(devices.reshape(shape), ("x", "z", "own"))


def solution(mesh):
    grid = split_mesh(mesh)
    data = ("x", "z")
    in_specs = (
        P(data, None, None, "own"),
        P(),
        P(data, None, None, "own"),
        P(data, None, None, "own"),
    )
    out_specs = (P(data, None, None, "own"), P(data, None, None, "own"), P(None, None, "own"))
    return jax.shard_map(
        on_device, mesh=grid, in_specs=in_specs, out_specs=out_specs, check_vma=False
    )
```
